512 devices in a mesh: harm: 16 (over y, x), tile: 32 (over z, core).
Axes of the slice: x: 4, y: 4, z: 16, core: 2. Of those that a mesh axis runs over, the one named last changes fastest.
Arguments:
- q_old: float32 [128, 10, 128, 256], P('harm', None, 'tile'), may hold values from -37 to 37
- base_rate: float32 [5, 128, 256], P(None, 'tile'), may hold values from 1 to 1.3
- freq_table: int32 [128], replicated, may hold values from 0 to 127, each once
- wall_flags: int32 [128], P('tile'), may hold values 0 or 1
Outputs:
- q_new: float32 [128, 10, 128, 256], P('harm', None, 'tile')
The draws below stay inside these ranges and needn't reach their ends.
Inputs may be any that keep to these rules, and one draw needn't show every extreme that they name: `freq_table`: each of 0 to 127 appears once.
All inputs are finite; a program needn't handle non-finite values. No bound on the sum of `wall_flags` on one device may be relied on, other than what follows from the above.
Results may differ from the reference program's by a relative error of at most 0.00017.
Values sent between devices are 32-bit elements; how exact they have to be, the bound alone decides.
No kernel may reach another device: no remote copies, remote signals or barrier semaphores. Data moves between devices by JAX's collectives and lax.ppermute only.
A program may use at most 64 MiB of HBM per device.

```python
import math
import jax
import jax.numpy as jnp
from jax import lax

HARMS = 128
VARS = 5
NZ = 256
ITERS = 2
SWEEPS = 4
NY = 128


def draw_q_old(key, part):
    key_noise = jax.random.fold_in(key, 11)
    key_harm = jax.random.fold_in(key, 12)
    key_cell = jax.random.fold_in(key, 13)
    noise = jax.random.normal(key_noise, (HARMS, 2 * VARS, NY, NZ), jnp.float32)
    noise = jnp.clip(noise, -4.0, 4.0)
    harm_scale = jnp.exp(jax.random.uniform(key_harm, (HARMS,), jnp.float32, math.log(0.3), math.log(3.0)))
    ramp = 0.5 + jnp.arange(NY, dtype=jnp.float32) / (NY - 1)
    cell_scale = ramp[:, None] * jnp.exp(jax.random.uniform(key_cell, (NY, NZ), jnp.float32, -0.7, 0.7))
    return noise * harm_scale[:, None, None, None] * cell_scale[None, None]


def set_ends(values, key, smallest, top_value):
    extent = values.shape
    place = [jax.random.randint(jax.random.fold_in(key, axis), (), 0, extent[axis]) for axis in range(len(extent))]
    values = values.at[tuple(place)].set(smallest)
    longest = extent.index(max(extent))
    place[longest] = (place[longest] + 1) % extent[longest]
    return values.at[tuple(place)].set(top_value)


def steps_of(rng, dims, shards, low, largest):
    loudness, own = 1.0, jax.random.fold_in(rng, 6)
    for dim, parts in shards:
        steps = jnp.exp(jax.random.uniform(jax.random.fold_in(own, dim), (parts,), jnp.float32, low / len(shards), largest / len(shards)))
        loudness = loudness * jnp.repeat(steps, dims[dim] // parts).reshape([-1 if axis == dim else 1 for axis in range(len(dims))])
    return loudness


def setup_inputs(seed: int = 0) -> dict:
    seeds = jax.random.split(jax.random.key(seed), 5)
    return {
        "q_old": draw_q_old(jax.random.fold_in(seeds[4], 71), 0),
        "base_rate": jnp.clip(jnp.exp(math.log(1.3) - 0.26236423 * jax.random.uniform(seeds[1], (VARS, NY, NZ), jnp.float32) ** steps_of(seeds[1], (VARS, NY, NZ), ((1, 32),), -0.2, 0.2)), 1.0, 1.3),
        "freq_table": jax.random.permutation(seeds[2], HARMS).astype(jnp.int32),
        "wall_flags": set_ends((jax.random.randint(seeds[3], (NY,), 0, 2) < 1).astype(jnp.int32), jax.random.fold_in(seeds[3], 1), 0, 1),
    }


coupling = 0.24
forcing_gain = 0.5
marching = 1.0
frequency_scale = 0.5

def build_tables(frequencies):
    harm_count = frequencies.shape[0]
    sample_count = 2 * harm_count
    sample_index = jnp.arange(sample_count, dtype=jnp.int32)
    phase_index = sample_index[:, None] * frequencies[None, :] % sample_count
    angles = phase_index.astype(jnp.float32) * (2.0 * math.pi / sample_count)
    pairs = jnp.stack([jnp.cos(angles), -jnp.sin(angles)], axis=2).reshape(sample_count, 2 * harm_count)
    forward = pairs / math.sqrt(harm_count)
    backward = pairs.T / math.sqrt(sample_count)
    return (forward, backward)

def spectral_forcing(coefficients, forward, backward):
    harm_count = coefficients.shape[0]
    var_count = coefficients.shape[1] // 2
    cell_count = coefficients.shape[2]
    stacked = coefficients.reshape(2 * harm_count, var_count * cell_count)
    samples = jnp.dot(forward, stacked, precision=lax.Precision.HIGHEST, preferred_element_type=jnp.float32)
    samples = samples.reshape(forward.shape[0], var_count, cell_count)
    product = jnp.roll(samples, -1, axis=1) * jnp.roll(samples, -2, axis=1)
    folded = jnp.dot(backward, product.reshape(forward.shape[0], var_count * cell_count), precision=lax.Precision.HIGHEST, preferred_element_type=jnp.float32)
    return folded.reshape(harm_count, 2 * var_count, cell_count)

def wall_ghost(iterate, wall_flags):
    edge = iterate[..., :1]
    return jnp.where(wall_flags[None, None, :, None] == 1, jnp.zeros_like(edge), edge)

def normal_sum(iterate, below_edge, above_edge):
    low_side = jnp.concatenate([below_edge, iterate[..., :-1]], axis=-1)
    high_side = jnp.concatenate([iterate[..., 1:], above_edge], axis=-1)
    return low_side + high_side

def relax(source, base_rate, frequency, beside):
    var_count = base_rate.shape[0]
    numerator = source + coupling * beside
    num_real = numerator[:, :var_count]
    num_imag = numerator[:, var_count:]
    rate_col = frequency[:, None, None, None]
    denominator = base_rate * base_rate + rate_col * rate_col
    new_real = (num_real * base_rate + num_imag * rate_col) / denominator
    new_imag = (num_imag * base_rate - num_real * rate_col) / denominator
    return jnp.concatenate([new_real, new_imag], axis=1)

def correction_terms(iterate, previous):
    var_count = previous.shape[1] // 2
    old_real = previous[:, :var_count]
    old_imag = previous[:, var_count:]
    it_real = iterate[:, :var_count]
    it_imag = iterate[:, var_count:]
    proj_real = lax.optimization_barrier(jnp.sum(old_real * it_real + old_imag * it_imag, axis=(1, 2, 3)))
    proj_imag = lax.optimization_barrier(jnp.sum(old_real * it_imag - old_imag * it_real, axis=(1, 2, 3)))
    norm_old = lax.optimization_barrier(jnp.sum(old_real * old_real + old_imag * old_imag, axis=(1, 2, 3)))
    return (proj_real, proj_imag, norm_old)

def apply_correction(iterate, previous, totals):
    proj_real, proj_imag, norm_old = totals
    var_count = previous.shape[1] // 2
    old_real = previous[:, :var_count]
    old_imag = previous[:, var_count:]
    shift_real = ((proj_real - norm_old) / norm_old)[:, None, None, None]
    shift_imag = (proj_imag / norm_old)[:, None, None, None]
    new_real = iterate[:, :var_count] - (shift_real * old_real - shift_imag * old_imag)
    new_imag = iterate[:, var_count:] - (shift_real * old_imag + shift_imag * old_real)
    return jnp.concatenate([new_real, new_imag], axis=1)

def reference(q_old, base_rate, freq_table, wall_flags):
    forward, backward = build_tables(freq_table)
    frequency = freq_table.astype(jnp.float32) * (frequency_scale / freq_table.shape[0])
    field = q_old
    harm_count, chan_count, row_count, depth = q_old.shape
    for outer_step in range(ITERS):
        forcing = spectral_forcing(field.reshape(harm_count, chan_count, row_count * depth), forward, backward)
        forcing = forcing.reshape(harm_count, chan_count, row_count, depth)
        source = marching * q_old + forcing_gain * forcing
        iterate = field
        for sweep_step in range(SWEEPS):
            beside = jnp.roll(iterate, 1, axis=2) + jnp.roll(iterate, -1, axis=2)
            beside = beside + normal_sum(iterate, wall_ghost(iterate, wall_flags), jnp.zeros_like(iterate[..., :1]))
            iterate = relax(source, base_rate, frequency, beside)
        field = apply_correction(iterate, q_old, correction_terms(iterate, q_old))
    return field
```

```python
import math

import jax
import jax.numpy as jnp
from jax import lax
from jax.sharding import PartitionSpec as P

ITERS = 2
SWEEPS = 4


coupling = 0.24
forcing_gain = 0.5
marching = 1.0
frequency_scale = 0.5


def extended(cells, sides, width):
    for axis, dim in sides:
        count = lax.axis_size(axis)
        head = lax.slice_in_dim(cells, 0, width, axis=dim)
        tail = lax.slice_in_dim(cells, cells.shape[dim] - width, cells.shape[dim], axis=dim)
        cells = jnp.concatenate(
            [
                lax.ppermute(tail, axis, [(i, (i + 1) % count) for i in range(count)]),
                cells,
                lax.ppermute(head, axis, [((i + 1) % count, i) for i in range(count)]),
            ],
            axis=dim,
        )
    return cells


def tile_sum(values, axis):
    count = lax.axis_size(axis)
    if count & (count - 1):
        return lax.psum(values, axis)
    step = 1
    while step < count:
        values = values + lax.ppermute(values, axis, [(i, i ^ step) for i in range(count)])
        step *= 2
    return values


def build_tables(frequencies):
    harm_count = frequencies.shape[0]
    sample_count = 2 * harm_count
    sample_index = jnp.arange(sample_count, dtype=jnp.int32)
    phase_index = sample_index[:, None] * frequencies[None, :] % sample_count
    angles = phase_index.astype(jnp.float32) * (2.0 * math.pi / sample_count)
    pairs = jnp.stack([jnp.cos(angles), -jnp.sin(angles)], axis=2).reshape(
        sample_count, 2 * harm_count
    )
    forward = pairs / math.sqrt(harm_count)
    backward = pairs.T / math.sqrt(sample_count)
    return (forward, backward)


def spectral_forcing(coefficients, forward, backward):
    harm_count = coefficients.shape[0]
    var_count = coefficients.shape[1] // 2
    cell_count = coefficients.shape[2]
    stacked = coefficients.reshape(2 * harm_count, var_count * cell_count)
    samples = jnp.dot(
        forward, stacked, precision=lax.Precision.HIGHEST, preferred_element_type=jnp.float32
    )
    samples = samples.reshape(forward.shape[0], var_count, cell_count)
    product = jnp.roll(samples, -1, axis=1) * jnp.roll(samples, -2, axis=1)
    folded = jnp.dot(
        backward,
        product.reshape(forward.shape[0], var_count * cell_count),
        precision=lax.Precision.HIGHEST,
        preferred_element_type=jnp.float32,
    )
    return folded.reshape(harm_count, 2 * var_count, cell_count)


def normal_sum(iterate, below_edge, above_edge):
    low_side = jnp.concatenate([below_edge, iterate[..., :-1]], axis=-1)
    high_side = jnp.concatenate([iterate[..., 1:], above_edge], axis=-1)
    return low_side + high_side


def relax(source, base_rate, frequency, beside):
    var_count = base_rate.shape[0]
    numerator = source + coupling * beside
    num_real = numerator[:, :var_count]
    num_imag = numerator[:, var_count:]
    rate_col = frequency[:, None, None, None]
    denominator = base_rate * base_rate + rate_col * rate_col
    new_real = (num_real * base_rate + num_imag * rate_col) / denominator
    new_imag = (num_imag * base_rate - num_real * rate_col) / denominator
    return jnp.concatenate([new_real, new_imag], axis=1)


def correction_terms(iterate, previous):
    var_count = previous.shape[1] // 2
    old_real = previous[:, :var_count]
    old_imag = previous[:, var_count:]
    it_real = iterate[:, :var_count]
    it_imag = iterate[:, var_count:]
    proj_real = jnp.sum(old_real * it_real + old_imag * it_imag, axis=(1, 2, 3))
    proj_imag = jnp.sum(old_real * it_imag - old_imag * it_real, axis=(1, 2, 3))
    norm_old = jnp.sum(old_real * old_real + old_imag * old_imag, axis=(1, 2, 3))
    return (proj_real, proj_imag, norm_old)


def apply_correction(iterate, previous, totals):
    proj_real, proj_imag, norm_old = totals
    var_count = previous.shape[1] // 2
    old_real = previous[:, :var_count]
    old_imag = previous[:, var_count:]
    shift_real = ((proj_real - norm_old) / norm_old)[:, None, None, None]
    shift_imag = (proj_imag / norm_old)[:, None, None, None]
    new_real = iterate[:, :var_count] - (shift_real * old_real - shift_imag * old_imag)
    new_imag = iterate[:, var_count:] - (shift_real * old_imag + shift_imag * old_real)
    return jnp.concatenate([new_real, new_imag], axis=1)


def shards(q_old, base_rate, freq_table, wall_flags):
    forward, backward = build_tables(freq_table)
    frequency_all = freq_table.astype(jnp.float32) * (frequency_scale / freq_table.shape[0])
    harm_rank = lax.axis_index("harm")
    local_harms = q_old.shape[0]
    frequency = lax.dynamic_slice_in_dim(frequency_all, harm_rank * local_harms, local_harms)
    keep_mask = (1 - wall_flags).astype(jnp.float32)[None, None, :, None]
    field = q_old
    for outer_step in range(ITERS):
        slab_block = lax.all_to_all(field, "harm", split_axis=3, concat_axis=0, tiled=True)
        harm_count, chan_count, row_count, depth = slab_block.shape
        forced = spectral_forcing(
            slab_block.reshape(harm_count, chan_count, row_count * depth), forward, backward
        )
        forced = forced.reshape(harm_count, chan_count, row_count, depth)
        forcing = lax.all_to_all(forced, "harm", split_axis=0, concat_axis=3, tiled=True)
        source = marching * q_old + forcing_gain * forcing
        iterate = field
        for sweep_step in range(SWEEPS):
            span_padded = extended(iterate, (("tile", 2),), 1)
            beside = span_padded[:, :, :-2] + span_padded[:, :, 2:]
            beside = beside + normal_sum(
                iterate, iterate[..., :1] * keep_mask, jnp.zeros_like(iterate[..., :1])
            )
            iterate = relax(source, base_rate, frequency, beside)
        totals = tile_sum(jnp.stack(correction_terms(iterate, q_old)), "tile")
        field = apply_correction(iterate, q_old, totals)
    return field


def solution(mesh):
    placed = (P("harm", None, "tile", None), P(None, "tile", None), P(), P("tile"))
    return jax.shard_map(
        shards, mesh=mesh, in_specs=placed, out_specs=P("harm", None, "tile", None), check_vma=False
    )
```

```python
import math

import jax
import jax.numpy as jnp
from jax import lax
from jax.sharding import PartitionSpec as P

ITERS = 2
SWEEPS = 4


coupling = 0.24
forcing_gain = 0.5
marching = 1.0
frequency_scale = 0.5


def extended(cells, sides, width):
    for axis, dim in sides:
        count = lax.axis_size(axis)
        head = lax.slice_in_dim(cells, 0, width, axis=dim)
        tail = lax.slice_in_dim(cells, cells.shape[dim] - width, cells.shape[dim], axis=dim)
        cells = jnp.concatenate(
            [
                lax.ppermute(tail, axis, [(i, (i + 1) % count) for i in range(count)]),
                cells,
                lax.ppermute(head, axis, [((i + 1) % count, i) for i in range(count)]),
            ],
            axis=dim,
        )
    return cells


def build_tables(frequencies):
    harm_count = frequencies.shape[0]
    sample_count = 2 * harm_count
    sample_index = jnp.arange(sample_count, dtype=jnp.int32)
    phase_index = sample_index[:, None] * frequencies[None, :] % sample_count
    angles = phase_index.astype(jnp.float32) * (2.0 * math.pi / sample_count)
    pairs = jnp.stack([jnp.cos(angles), -jnp.sin(angles)], axis=2).reshape(
        sample_count, 2 * harm_count
    )
    forward = pairs / math.sqrt(harm_count)
    backward = pairs.T / math.sqrt(sample_count)
    return (forward, backward)


def spectral_forcing(coefficients, forward, backward):
    harm_count = coefficients.shape[0]
    var_count = coefficients.shape[1] // 2
    cell_count = coefficients.shape[2]
    stacked = coefficients.reshape(2 * harm_count, var_count * cell_count)
    samples = jnp.dot(
        forward, stacked, precision=lax.Precision.HIGHEST, preferred_element_type=jnp.float32
    )
    samples = samples.reshape(forward.shape[0], var_count, cell_count)
    product = jnp.roll(samples, -1, axis=1) * jnp.roll(samples, -2, axis=1)
    folded = jnp.dot(
        backward,
        product.reshape(forward.shape[0], var_count * cell_count),
        precision=lax.Precision.HIGHEST,
        preferred_element_type=jnp.float32,
    )
    return folded.reshape(harm_count, 2 * var_count, cell_count)


def normal_sum(iterate, below_edge, above_edge):
    low_side = jnp.concatenate([below_edge, iterate[..., :-1]], axis=-1)
    high_side = jnp.concatenate([iterate[..., 1:], above_edge], axis=-1)
    return low_side + high_side


def relax(source, base_rate, frequency, beside):
    var_count = base_rate.shape[0]
    numerator = source + coupling * beside
    num_real = numerator[:, :var_count]
    num_imag = numerator[:, var_count:]
    rate_col = frequency[:, None, None, None]
    denominator = base_rate * base_rate + rate_col * rate_col
    new_real = (num_real * base_rate + num_imag * rate_col) / denominator
    new_imag = (num_imag * base_rate - num_real * rate_col) / denominator
    return jnp.concatenate([new_real, new_imag], axis=1)


def correction_terms(iterate, previous):
    var_count = previous.shape[1] // 2
    old_real = previous[:, :var_count]
    old_imag = previous[:, var_count:]
    it_real = iterate[:, :var_count]
    it_imag = iterate[:, var_count:]
    proj_real = jnp.sum(old_real * it_real + old_imag * it_imag, axis=(1, 2, 3))
    proj_imag = jnp.sum(old_real * it_imag - old_imag * it_real, axis=(1, 2, 3))
    norm_old = jnp.sum(old_real * old_real + old_imag * old_imag, axis=(1, 2, 3))
    return (proj_real, proj_imag, norm_old)


def apply_correction(iterate, previous, totals):
    proj_real, proj_imag, norm_old = totals
    var_count = previous.shape[1] // 2
    old_real = previous[:, :var_count]
    old_imag = previous[:, var_count:]
    shift_real = ((proj_real - norm_old) / norm_old)[:, None, None, None]
    shift_imag = (proj_imag / norm_old)[:, None, None, None]
    new_real = iterate[:, :var_count] - (shift_real * old_real - shift_imag * old_imag)
    new_imag = iterate[:, var_count:] - (shift_real * old_imag + shift_imag * old_real)
    return jnp.concatenate([new_real, new_imag], axis=1)


def tile_sum(values, axis):
    count = lax.axis_size(axis)
    spread = jnp.broadcast_to(values[None], (count,) + values.shape)
    return lax.all_to_all(spread, axis, 0, 0, tiled=True).sum(axis=0)


def spectral_slabs(field, forward, backward):
    harms, chans, rows, depth = field.shape
    groups = lax.axis_size("harm")
    width = depth // groups
    var_count = chans // 2
    cols = field.reshape(harms * chans * rows, depth).T.reshape(groups, width, harms * chans * rows)
    slabs = lax.all_to_all(cols, "harm", 0, 0, tiled=True)
    slabs = slabs.reshape(groups, width, harms, 2, var_count, rows)
    samples = jnp.einsum(
        "mshp,szhpvy->mvyz",
        forward.reshape(forward.shape[0], groups, harms, 2),
        slabs,
        precision=lax.Precision.HIGHEST,
        preferred_element_type=jnp.float32,
    )
    product = jnp.roll(samples, -1, axis=1) * jnp.roll(samples, -2, axis=1)
    folded = jnp.einsum(
        "shpm,mvyz->szhpvy",
        backward.reshape(groups, harms, 2, backward.shape[1]),
        product,
        precision=lax.Precision.HIGHEST,
        preferred_element_type=jnp.float32,
    )
    back = lax.all_to_all(folded.reshape(groups, width, harms * chans * rows), "harm", 0, 0, tiled=True)
    return back.reshape(depth, harms * chans * rows).T.reshape(harms, chans, rows, depth)


def shards(q_old, base_rate, freq_table, wall_flags):
    forward, backward = build_tables(freq_table)
    frequency_all = freq_table.astype(jnp.float32) * (frequency_scale / freq_table.shape[0])
    harm_rank = lax.axis_index("harm")
    local_harms = q_old.shape[0]
    frequency = lax.dynamic_slice_in_dim(frequency_all, harm_rank * local_harms, local_harms)
    keep_mask = (1 - wall_flags).astype(jnp.float32)[None, None, :, None]
    field = q_old
    for outer_step in range(ITERS):
        forcing = spectral_slabs(field, forward, backward)
        source = marching * q_old + forcing_gain * forcing
        iterate = field
        for sweep_step in range(SWEEPS):
            span_padded = extended(iterate, (("tile", 2),), 1)
            beside = span_padded[:, :, :-2] + span_padded[:, :, 2:]
            beside = beside + normal_sum(
                iterate, iterate[..., :1] * keep_mask, jnp.zeros_like(iterate[..., :1])
            )
            iterate = relax(source, base_rate, frequency, beside)
        totals = tile_sum(jnp.stack(correction_terms(iterate, q_old)), "tile")
        field = apply_correction(iterate, q_old, totals)
    return field


def solution(mesh):
    placed = (P("harm", None, "tile", None), P(None, "tile", None), P(), P("tile"))
    return jax.shard_map(
        shards, mesh=mesh, in_specs=placed, out_specs=P("harm", None, "tile", None), check_vma=False
    )
```

```python
import math

import jax
import jax.numpy as jnp
from jax import lax
from jax.sharding import PartitionSpec as P

ITERS = 2
SWEEPS = 4


coupling = 0.24
forcing_gain = 0.5
marching = 1.0
frequency_scale = 0.5


def extended(cells, sides, width):
    for axis, dim in sides:
        count = lax.axis_size(axis)
        head = lax.slice_in_dim(cells, 0, width, axis=dim)
        tail = lax.slice_in_dim(cells, cells.shape[dim] - width, cells.shape[dim], axis=dim)
        cells = jnp.concatenate(
            [
                lax.ppermute(tail, axis, [(i, (i + 1) % count) for i in range(count)]),
                cells,
                lax.ppermute(head, axis, [((i + 1) % count, i) for i in range(count)]),
            ],
            axis=dim,
        )
    return cells


def build_tables(frequencies):
    harm_count = frequencies.shape[0]
    sample_count = 2 * harm_count
    sample_index = jnp.arange(sample_count, dtype=jnp.int32)
    phase_index = sample_index[:, None] * frequencies[None, :] % sample_count
    angles = phase_index.astype(jnp.float32) * (2.0 * math.pi / sample_count)
    pairs = jnp.stack([jnp.cos(angles), -jnp.sin(angles)], axis=2).reshape(
        sample_count, 2 * harm_count
    )
    forward = pairs / math.sqrt(harm_count)
    backward = pairs.T / math.sqrt(sample_count)
    return (forward, backward)


def spectral_forcing(coefficients, forward, backward):
    harm_count = coefficients.shape[0]
    var_count = coefficients.shape[1] // 2
    cell_count = coefficients.shape[2]
    stacked = coefficients.reshape(2 * harm_count, var_count * cell_count)
    samples = jnp.dot(
        forward, stacked, precision=lax.Precision.HIGHEST, preferred_element_type=jnp.float32
    )
    samples = samples.reshape(forward.shape[0], var_count, cell_count)
    product = jnp.roll(samples, -1, axis=1) * jnp.roll(samples, -2, axis=1)
    folded = jnp.dot(
        backward,
        product.reshape(forward.shape[0], var_count * cell_count),
        precision=lax.Precision.HIGHEST,
        preferred_element_type=jnp.float32,
    )
    return folded.reshape(harm_count, 2 * var_count, cell_count)


def normal_sum(iterate, below_edge, above_edge):
    low_side = jnp.concatenate([below_edge, iterate[..., :-1]], axis=-1)
    high_side = jnp.concatenate([iterate[..., 1:], above_edge], axis=-1)
    return low_side + high_side


def relax(source, base_rate, frequency, beside):
    var_count = base_rate.shape[0]
    numerator = source + coupling * beside
    num_real = numerator[:, :var_count]
    num_imag = numerator[:, var_count:]
    rate_col = frequency[:, None, None, None]
    denominator = base_rate * base_rate + rate_col * rate_col
    new_real = (num_real * base_rate + num_imag * rate_col) / denominator
    new_imag = (num_imag * base_rate - num_real * rate_col) / denominator
    return jnp.concatenate([new_real, new_imag], axis=1)


def correction_terms(iterate, previous):
    var_count = previous.shape[1] // 2
    old_real = previous[:, :var_count]
    old_imag = previous[:, var_count:]
    it_real = iterate[:, :var_count]
    it_imag = iterate[:, var_count:]
    proj_real = jnp.sum(old_real * it_real + old_imag * it_imag, axis=(1, 2, 3))
    proj_imag = jnp.sum(old_real * it_imag - old_imag * it_real, axis=(1, 2, 3))
    norm_old = jnp.sum(old_real * old_real + old_imag * old_imag, axis=(1, 2, 3))
    return (proj_real, proj_imag, norm_old)


def apply_correction(iterate, previous, totals):
    proj_real, proj_imag, norm_old = totals
    var_count = previous.shape[1] // 2
    old_real = previous[:, :var_count]
    old_imag = previous[:, var_count:]
    shift_real = ((proj_real - norm_old) / norm_old)[:, None, None, None]
    shift_imag = (proj_imag / norm_old)[:, None, None, None]
    new_real = iterate[:, :var_count] - (shift_real * old_real - shift_imag * old_imag)
    new_imag = iterate[:, var_count:] - (shift_real * old_imag + shift_imag * old_real)
    return jnp.concatenate([new_real, new_imag], axis=1)


def tile_sum(values, axis):
    count = lax.axis_size(axis)
    spread = jnp.broadcast_to(values[None], (count,) + values.shape)
    return lax.all_to_all(spread, axis, 0, 0, tiled=True).sum(axis=0)


def spectral_slabs(field, forward, backward):
    harms, chans, rows, depth = field.shape
    groups = lax.axis_size("harm")
    width = depth // groups
    var_count = chans // 2
    cols = field.reshape(harms * chans * rows, depth).T.reshape(groups, width, harms * chans * rows)
    slabs = lax.all_to_all(cols, "harm", 0, 0, tiled=True)
    slabs = slabs.reshape(groups, width, harms, 2, var_count, rows)
    samples = jnp.einsum(
        "mshp,szhpvy->mvyz",
        forward.reshape(forward.shape[0], groups, harms, 2),
        slabs,
        precision=lax.Precision.HIGHEST,
        preferred_element_type=jnp.float32,
    )
    product = jnp.roll(samples, -1, axis=1) * jnp.roll(samples, -2, axis=1)
    folded = jnp.einsum(
        "shpm,mvyz->szhpvy",
        backward.reshape(groups, harms, 2, backward.shape[1]),
        product,
        precision=lax.Precision.HIGHEST,
        preferred_element_type=jnp.float32,
    )
    back = lax.all_to_all(folded.reshape(groups, width, harms * chans * rows), "harm", 0, 0, tiled=True)
    return back.reshape(depth, harms * chans * rows).T.reshape(harms, chans, rows, depth)


def span_halo(block, width):
    count = lax.axis_size("tile")
    rows = block.shape[-2]
    from_left = lax.ppermute(
        block[..., rows - width :, :], "tile", [(i, (i + 1) % count) for i in range(count)]
    )
    from_right = lax.ppermute(block[..., :width, :], "tile", [((i + 1) % count, i) for i in range(count)])
    return from_left, from_right


def with_halo(block, halo):
    return jnp.concatenate([halo[0], block, halo[1]], axis=-2)


def sweep(iterate, source, base_rate, keep, frequency):
    center = iterate[:, :, 1:-1]
    beside = iterate[:, :, :-2] + iterate[:, :, 2:]
    beside = beside + normal_sum(center, center[..., :1] * keep, jnp.zeros_like(center[..., :1]))
    return relax(source, base_rate, frequency, beside)


def shards(q_old, base_rate, freq_table, wall_flags):
    forward, backward = build_tables(freq_table)
    frequency_all = freq_table.astype(jnp.float32) * (frequency_scale / freq_table.shape[0])
    harm_rank = lax.axis_index("harm")
    local_harms = q_old.shape[0]
    frequency = lax.dynamic_slice_in_dim(frequency_all, harm_rank * local_harms, local_harms)
    rows = q_old.shape[2]
    assert rows >= SWEEPS
    keep = (1 - wall_flags).astype(jnp.float32)[:, None]
    keep_ext = with_halo(keep, span_halo(keep, SWEEPS))[None, None]
    base_ext = with_halo(base_rate, span_halo(base_rate, SWEEPS))
    q_halo = span_halo(q_old, SWEEPS)
    q_ext = with_halo(q_old, q_halo)
    field = q_old
    field_ext = q_ext
    for outer_step in range(ITERS):
        forcing = spectral_slabs(field, forward, backward)
        forcing_ext = with_halo(forcing, span_halo(forcing, SWEEPS - 1))
        source_ext = marching * q_ext[:, :, 1:-1] + forcing_gain * forcing_ext
        iterate = field_ext
        for sweep_step in range(1, SWEEPS + 1):
            low, high = sweep_step, rows + 2 * SWEEPS - sweep_step
            iterate = sweep(
                iterate,
                source_ext[:, :, low - 1 : high - 1],
                base_ext[:, low:high],
                keep_ext[:, :, low:high],
                frequency,
            )
        last = outer_step == ITERS - 1
        if not last:
            it_halo = span_halo(iterate, SWEEPS)
        totals = tile_sum(jnp.stack(correction_terms(iterate, q_old)), "tile")
        field = apply_correction(iterate, q_old, totals)
        if not last:
            field_ext = jnp.concatenate(
                [
                    apply_correction(it_halo[0], q_halo[0], totals),
                    field,
                    apply_correction(it_halo[1], q_halo[1], totals),
                ],
                axis=2,
            )
    return field


def solution(mesh):
    placed = (P("harm", None, "tile", None), P(None, "tile", None), P(), P("tile"))
    return jax.shard_map(
        shards, mesh=mesh, in_specs=placed, out_specs=P("harm", None, "tile", None), check_vma=False
    )
```

```python
import math

import jax
import jax.numpy as jnp
from jax import lax
from jax.sharding import Mesh, PartitionSpec as P

ITERS = 2
SWEEPS = 4
TILE = ("z", "core")


coupling = 0.24
forcing_gain = 0.5
marching = 1.0
frequency_scale = 0.5


def build_tables(frequencies):
    harm_count = frequencies.shape[0]
    sample_count = 2 * harm_count
    sample_index = jnp.arange(sample_count, dtype=jnp.int32)
    phase_index = sample_index[:, None] * frequencies[None, :] % sample_count
    angles = phase_index.astype(jnp.float32) * (2.0 * math.pi / sample_count)
    pairs = jnp.stack([jnp.cos(angles), -jnp.sin(angles)], axis=2).reshape(
        sample_count, 2 * harm_count
    )
    forward = pairs / math.sqrt(harm_count)
    backward = pairs.T / math.sqrt(sample_count)
    return (forward, backward)


def spectral_forcing(coefficients, forward, backward):
    harm_count = coefficients.shape[0]
    var_count = coefficients.shape[1] // 2
    cell_count = coefficients.shape[2]
    stacked = coefficients.reshape(2 * harm_count, var_count * cell_count)
    samples = jnp.dot(
        forward, stacked, precision=lax.Precision.HIGHEST, preferred_element_type=jnp.float32
    )
    samples = samples.reshape(forward.shape[0], var_count, cell_count)
    product = jnp.roll(samples, -1, axis=1) * jnp.roll(samples, -2, axis=1)
    folded = jnp.dot(
        backward,
        product.reshape(forward.shape[0], var_count * cell_count),
        precision=lax.Precision.HIGHEST,
        preferred_element_type=jnp.float32,
    )
    return folded.reshape(harm_count, 2 * var_count, cell_count)


def normal_sum(iterate, below_edge, above_edge):
    low_side = jnp.concatenate([below_edge, iterate[..., :-1]], axis=-1)
    high_side = jnp.concatenate([iterate[..., 1:], above_edge], axis=-1)
    return low_side + high_side


def relax(source, base_rate, frequency, beside):
    var_count = base_rate.shape[0]
    numerator = source + coupling * beside
    num_real = numerator[:, :var_count]
    num_imag = numerator[:, var_count:]
    rate_col = frequency[:, None, None, None]
    denominator = base_rate * base_rate + rate_col * rate_col
    new_real = (num_real * base_rate + num_imag * rate_col) / denominator
    new_imag = (num_imag * base_rate - num_real * rate_col) / denominator
    return jnp.concatenate([new_real, new_imag], axis=1)


def correction_terms(iterate, previous):
    var_count = previous.shape[1] // 2
    old_real = previous[:, :var_count]
    old_imag = previous[:, var_count:]
    it_real = iterate[:, :var_count]
    it_imag = iterate[:, var_count:]
    proj_real = jnp.sum(old_real * it_real + old_imag * it_imag, axis=(1, 2, 3))
    proj_imag = jnp.sum(old_real * it_imag - old_imag * it_real, axis=(1, 2, 3))
    norm_old = jnp.sum(old_real * old_real + old_imag * old_imag, axis=(1, 2, 3))
    return (proj_real, proj_imag, norm_old)


def apply_correction(iterate, previous, totals):
    proj_real, proj_imag, norm_old = totals
    var_count = previous.shape[1] // 2
    old_real = previous[:, :var_count]
    old_imag = previous[:, var_count:]
    shift_real = ((proj_real - norm_old) / norm_old)[:, None, None, None]
    shift_imag = (proj_imag / norm_old)[:, None, None, None]
    new_real = iterate[:, :var_count] - (shift_real * old_real - shift_imag * old_imag)
    new_imag = iterate[:, var_count:] - (shift_real * old_imag + shift_imag * old_real)
    return jnp.concatenate([new_real, new_imag], axis=1)


def tile_sum(values):
    values = values + lax.ppermute(values, "core", [(0, 1), (1, 0)])
    count = lax.axis_size("z")
    spread = jnp.broadcast_to(values[None], (count,) + values.shape)
    return lax.all_to_all(spread, "z", 0, 0, tiled=True).sum(axis=0)


def spectral_slabs(field, forward, backward):
    harms, chans, rows, depth = field.shape
    groups = lax.axis_size("harm")
    width = depth // groups
    var_count = chans // 2
    cols = field.reshape(harms * chans * rows, depth).T.reshape(groups, width, harms * chans * rows)
    slabs = lax.all_to_all(cols, "harm", 0, 0, tiled=True)
    slabs = slabs.reshape(groups, width, harms, 2, var_count, rows)
    samples = jnp.einsum(
        "mshp,szhpvy->mvyz",
        forward.reshape(forward.shape[0], groups, harms, 2),
        slabs,
        precision=lax.Precision.HIGHEST,
        preferred_element_type=jnp.float32,
    )
    product = jnp.roll(samples, -1, axis=1) * jnp.roll(samples, -2, axis=1)
    folded = jnp.einsum(
        "shpm,mvyz->szhpvy",
        backward.reshape(groups, harms, 2, backward.shape[1]),
        product,
        precision=lax.Precision.HIGHEST,
        preferred_element_type=jnp.float32,
    )
    back = lax.all_to_all(folded.reshape(groups, width, harms * chans * rows), "harm", 0, 0, tiled=True)
    return back.reshape(depth, harms * chans * rows).T.reshape(harms, chans, rows, depth)


def span_halo(blocks, width):
    count = lax.axis_size(TILE)
    rows = [block.shape[-2] for block in blocks]
    if len(blocks) == 1:
        low, high = blocks[0][..., rows[0] - width :, :], blocks[0][..., :width, :]
        return [
            (
                lax.ppermute(low, TILE, [(i, (i + 1) % count) for i in range(count)]),
                lax.ppermute(high, TILE, [((i + 1) % count, i) for i in range(count)]),
            )
        ]
    lows = jnp.concatenate([b[..., r - width :, :].reshape(-1) for b, r in zip(blocks, rows)])
    highs = jnp.concatenate([b[..., :width, :].reshape(-1) for b in blocks])
    from_left = lax.ppermute(lows, TILE, [(i, (i + 1) % count) for i in range(count)])
    from_right = lax.ppermute(highs, TILE, [((i + 1) % count, i) for i in range(count)])
    halos, offset = [], 0
    for b in blocks:
        shape = b.shape[:-2] + (width,) + b.shape[-1:]
        size = math.prod(shape)
        halos.append((from_left[offset : offset + size].reshape(shape), from_right[offset : offset + size].reshape(shape)))
        offset += size
    return halos


def with_halo(block, halo):
    return jnp.concatenate([halo[0], block, halo[1]], axis=-2)


def sweep(iterate, source, base_rate, keep, frequency):
    center = iterate[:, :, 1:-1]
    beside = iterate[:, :, :-2] + iterate[:, :, 2:]
    beside = beside + normal_sum(center, center[..., :1] * keep, jnp.zeros_like(center[..., :1]))
    return relax(source, base_rate, frequency, beside)


def shards(q_old, base_rate, freq_table, wall_flags):
    forward, backward = build_tables(freq_table)
    frequency_all = freq_table.astype(jnp.float32) * (frequency_scale / freq_table.shape[0])
    harm_rank = lax.axis_index("harm")
    local_harms = q_old.shape[0]
    frequency = lax.dynamic_slice_in_dim(frequency_all, harm_rank * local_harms, local_harms)
    rows = q_old.shape[2]
    assert rows >= SWEEPS
    keep = (1 - wall_flags).astype(jnp.float32)[:, None]
    q_halo, base_halo, keep_halo = span_halo((q_old, base_rate, keep), SWEEPS)
    keep_ext = with_halo(keep, keep_halo)[None, None]
    base_ext = with_halo(base_rate, base_halo)
    q_ext = with_halo(q_old, q_halo)
    field = q_old
    field_ext = q_ext
    for outer_step in range(ITERS):
        forcing = spectral_slabs(field, forward, backward)
        forcing_ext = with_halo(forcing, span_halo((forcing,), SWEEPS - 1)[0])
        source_ext = marching * q_ext[:, :, 1:-1] + forcing_gain * forcing_ext
        iterate = field_ext
        for sweep_step in range(1, SWEEPS + 1):
            low, high = sweep_step, rows + 2 * SWEEPS - sweep_step
            iterate = sweep(
                iterate,
                source_ext[:, :, low - 1 : high - 1],
                base_ext[:, low:high],
                keep_ext[:, :, low:high],
                frequency,
            )
        last = outer_step == ITERS - 1
        if not last:
            (it_halo,) = span_halo((iterate,), SWEEPS)
        totals = tile_sum(jnp.stack(correction_terms(iterate, q_old)))
        field = apply_correction(iterate, q_old, totals)
        if not last:
            field_ext = jnp.concatenate(
                [
                    apply_correction(it_halo[0], q_halo[0], totals),
                    field,
                    apply_correction(it_halo[1], q_halo[1], totals),
                ],
                axis=2,
            )
    return field


def solution(mesh):
    harms, tiles = mesh.devices.shape
    split = Mesh(mesh.devices.reshape(harms, tiles // 2, 2), ("harm", "z", "core"))
    placed = (P("harm", None, TILE, None), P(None, TILE, None), P(), P(TILE))
    return jax.shard_map(
        shards, mesh=split, in_specs=placed, out_specs=P("harm", None, TILE, None), check_vma=False
    )
```

```python
import math

import jax
import jax.numpy as jnp
from jax import lax
from jax.sharding import Mesh, PartitionSpec as P

ITERS = 2
SWEEPS = 4
TILE = ("z", "core")


coupling = 0.24
forcing_gain = 0.5
marching = 1.0
frequency_scale = 0.5


def build_tables(frequencies):
    harm_count = frequencies.shape[0]
    sample_count = 2 * harm_count
    sample_index = jnp.arange(sample_count, dtype=jnp.int32)
    phase_index = sample_index[:, None] * frequencies[None, :] % sample_count
    angles = phase_index.astype(jnp.float32) * (2.0 * math.pi / sample_count)
    pairs = jnp.stack([jnp.cos(angles), -jnp.sin(angles)], axis=2).reshape(
        sample_count, 2 * harm_count
    )
    forward = pairs / math.sqrt(harm_count)
    backward = pairs.T / math.sqrt(sample_count)
    return (forward, backward)


def spectral_forcing(coefficients, forward, backward):
    harm_count = coefficients.shape[0]
    var_count = coefficients.shape[1] // 2
    cell_count = coefficients.shape[2]
    stacked = coefficients.reshape(2 * harm_count, var_count * cell_count)
    samples = jnp.dot(
        forward, stacked, precision=lax.Precision.HIGHEST, preferred_element_type=jnp.float32
    )
    samples = samples.reshape(forward.shape[0], var_count, cell_count)
    product = jnp.roll(samples, -1, axis=1) * jnp.roll(samples, -2, axis=1)
    folded = jnp.dot(
        backward,
        product.reshape(forward.shape[0], var_count * cell_count),
        precision=lax.Precision.HIGHEST,
        preferred_element_type=jnp.float32,
    )
    return folded.reshape(harm_count, 2 * var_count, cell_count)


def normal_sum(iterate, below_edge, above_edge):
    low_side = jnp.concatenate([below_edge, iterate[..., :-1]], axis=-1)
    high_side = jnp.concatenate([iterate[..., 1:], above_edge], axis=-1)
    return low_side + high_side


def relax(source, base_rate, frequency, beside):
    var_count = base_rate.shape[0]
    numerator = source + coupling * beside
    num_real = numerator[:, :var_count]
    num_imag = numerator[:, var_count:]
    rate_col = frequency[:, None, None, None]
    denominator = base_rate * base_rate + rate_col * rate_col
    new_real = (num_real * base_rate + num_imag * rate_col) / denominator
    new_imag = (num_imag * base_rate - num_real * rate_col) / denominator
    return jnp.concatenate([new_real, new_imag], axis=1)


def correction_terms(iterate, previous):
    var_count = previous.shape[1] // 2
    old_real = previous[:, :var_count]
    old_imag = previous[:, var_count:]
    it_real = iterate[:, :var_count]
    it_imag = iterate[:, var_count:]
    proj_real = jnp.sum(old_real * it_real + old_imag * it_imag, axis=(1, 2, 3))
    proj_imag = jnp.sum(old_real * it_imag - old_imag * it_real, axis=(1, 2, 3))
    norm_old = jnp.sum(old_real * old_real + old_imag * old_imag, axis=(1, 2, 3))
    return (proj_real, proj_imag, norm_old)


def apply_correction(iterate, previous, totals):
    proj_real, proj_imag, norm_old = totals
    var_count = previous.shape[1] // 2
    old_real = previous[:, :var_count]
    old_imag = previous[:, var_count:]
    shift_real = ((proj_real - norm_old) / norm_old)[:, None, None, None]
    shift_imag = (proj_imag / norm_old)[:, None, None, None]
    new_real = iterate[:, :var_count] - (shift_real * old_real - shift_imag * old_imag)
    new_imag = iterate[:, var_count:] - (shift_real * old_imag + shift_imag * old_real)
    return jnp.concatenate([new_real, new_imag], axis=1)


def tile_sum(values):
    count = lax.axis_size(TILE)
    spread = jnp.broadcast_to(values[None], (count,) + values.shape)
    return lax.all_to_all(spread, TILE, 0, 0, tiled=True).sum(axis=0)


def spectral_slabs(field, forward, backward):
    harms, chans, rows, depth = field.shape
    groups = lax.axis_size("harm")
    width = depth // groups
    var_count = chans // 2
    cols = field.reshape(harms * chans * rows, depth).T.reshape(groups, width, harms * chans * rows)
    slabs = lax.all_to_all(cols, "harm", 0, 0, tiled=True)
    slabs = slabs.reshape(groups, width, harms, 2, var_count, rows)
    samples = jnp.einsum(
        "mshp,szhpvy->mvyz",
        forward.reshape(forward.shape[0], groups, harms, 2),
        slabs,
        precision=lax.Precision.HIGHEST,
        preferred_element_type=jnp.float32,
    )
    product = jnp.roll(samples, -1, axis=1) * jnp.roll(samples, -2, axis=1)
    folded = jnp.einsum(
        "shpm,mvyz->szhpvy",
        backward.reshape(groups, harms, 2, backward.shape[1]),
        product,
        precision=lax.Precision.HIGHEST,
        preferred_element_type=jnp.float32,
    )
    back = lax.all_to_all(folded.reshape(groups, width, harms * chans * rows), "harm", 0, 0, tiled=True)
    return back.reshape(depth, harms * chans * rows).T.reshape(harms, chans, rows, depth)


def span_halo(blocks, width):
    count = lax.axis_size(TILE)
    rows = [block.shape[-2] for block in blocks]
    if len(blocks) == 1:
        low, high = blocks[0][..., rows[0] - width :, :], blocks[0][..., :width, :]
        return [
            (
                lax.ppermute(low, TILE, [(i, (i + 1) % count) for i in range(count)]),
                lax.ppermute(high, TILE, [((i + 1) % count, i) for i in range(count)]),
            )
        ]
    lows = jnp.concatenate([b[..., r - width :, :].reshape(-1) for b, r in zip(blocks, rows)])
    highs = jnp.concatenate([b[..., :width, :].reshape(-1) for b in blocks])
    from_left = lax.ppermute(lows, TILE, [(i, (i + 1) % count) for i in range(count)])
    from_right = lax.ppermute(highs, TILE, [((i + 1) % count, i) for i in range(count)])
    halos, offset = [], 0
    for b in blocks:
        shape = b.shape[:-2] + (width,) + b.shape[-1:]
        size = math.prod(shape)
        halos.append((from_left[offset : offset + size].reshape(shape), from_right[offset : offset + size].reshape(shape)))
        offset += size
    return halos


def with_halo(block, halo):
    return jnp.concatenate([halo[0], block, halo[1]], axis=-2)


def sweep(iterate, source, base_rate, keep, frequency):
    center = iterate[:, :, 1:-1]
    beside = iterate[:, :, :-2] + iterate[:, :, 2:]
    beside = beside + normal_sum(center, center[..., :1] * keep, jnp.zeros_like(center[..., :1]))
    return relax(source, base_rate, frequency, beside)


def conj_gain(values, base_rate, frequency):
    var_count = base_rate.shape[0]
    rate_col = frequency[:, None, None, None]
    denominator = base_rate * base_rate + rate_col * rate_col
    real, imag = values[:, :var_count], values[:, var_count:]
    return jnp.concatenate(
        [(real * base_rate - imag * rate_col) / denominator, (imag * base_rate + real * rate_col) / denominator],
        axis=1,
    )


def adjoint_weights(q_ext, base_ext, keep_ext, frequency, rows):
    total = rows + 2 * SWEEPS
    weights = [q_ext]
    for step in range(1, SWEEPS + 1):
        low, high = step - 1, total - step + 1
        scaled = conj_gain(weights[-1], base_ext[:, low:high], frequency)
        center = scaled[:, :, 1:-1]
        beside = scaled[:, :, :-2] + scaled[:, :, 2:]
        beside = beside + normal_sum(
            center, center[..., :1] * keep_ext[:, :, step : total - step], jnp.zeros_like(center[..., :1])
        )
        weights.append(coupling * beside)
    local = [w[:, :, SWEEPS - j : SWEEPS - j + rows] for j, w in enumerate(weights)]
    summed = local[0]
    for w in local[1:SWEEPS]:
        summed = summed + w
    return local[SWEEPS], conj_gain(summed, base_ext[:, SWEEPS : SWEEPS + rows], frequency)


def shards(q_old, base_rate, freq_table, wall_flags):
    forward, backward = build_tables(freq_table)
    frequency_all = freq_table.astype(jnp.float32) * (frequency_scale / freq_table.shape[0])
    harm_rank = lax.axis_index("harm")
    local_harms = q_old.shape[0]
    frequency = lax.dynamic_slice_in_dim(frequency_all, harm_rank * local_harms, local_harms)
    rows = q_old.shape[2]
    assert rows >= SWEEPS
    keep = (1 - wall_flags).astype(jnp.float32)[:, None]
    q_halo, base_halo, keep_halo = span_halo((q_old, base_rate, keep), SWEEPS)
    keep_ext = with_halo(keep, keep_halo)[None, None]
    base_ext = with_halo(base_rate, base_halo)
    q_ext = with_halo(q_old, q_halo)
    field_weight, source_weight = adjoint_weights(q_ext, base_ext, keep_ext, frequency, rows)
    norm_old = correction_terms(q_old, q_old)[2]
    field = q_old
    field_ext = q_ext
    for outer_step in range(ITERS):
        field_proj = correction_terms(field, field_weight)
        forcing = spectral_slabs(field, forward, backward)
        source_proj = correction_terms(marching * q_old + forcing_gain * forcing, source_weight)
        totals = tile_sum(
            jnp.stack([field_proj[0] + source_proj[0], field_proj[1] + source_proj[1], norm_old])
        )
        forcing_ext = with_halo(forcing, span_halo((forcing,), SWEEPS - 1)[0])
        source_ext = marching * q_ext[:, :, 1:-1] + forcing_gain * forcing_ext
        iterate = field_ext
        for sweep_step in range(1, SWEEPS + 1):
            low, high = sweep_step, rows + 2 * SWEEPS - sweep_step
            iterate = sweep(
                iterate,
                source_ext[:, :, low - 1 : high - 1],
                base_ext[:, low:high],
                keep_ext[:, :, low:high],
                frequency,
            )
        last = outer_step == ITERS - 1
        if not last:
            (it_halo,) = span_halo((iterate,), SWEEPS)
        field = apply_correction(iterate, q_old, totals)
        if not last:
            field_ext = jnp.concatenate(
                [
                    apply_correction(it_halo[0], q_halo[0], totals),
                    field,
                    apply_correction(it_halo[1], q_halo[1], totals),
                ],
                axis=2,
            )
    return field


def solution(mesh):
    harms, tiles = mesh.devices.shape
    split = Mesh(mesh.devices.reshape(harms, tiles // 2, 2), ("harm", "z", "core"))
    placed = (P("harm", None, TILE, None), P(None, TILE, None), P(), P(TILE))
    return jax.shard_map(
        shards, mesh=split, in_specs=placed, out_specs=P("harm", None, TILE, None), check_vma=False
    )
```

```python
import math

import jax
import jax.numpy as jnp
from jax import lax
from jax.sharding import Mesh, PartitionSpec as P


ITERS = 2
SWEEPS = 4
TILE = ("z", "core")


coupling = 0.24
forcing_gain = 0.5
marching = 1.0
frequency_scale = 0.5


def build_tables(frequencies):
    harm_count = frequencies.shape[0]
    sample_count = 2 * harm_count
    sample_index = jnp.arange(sample_count, dtype=jnp.int32)
    phase_index = sample_index[:, None] * frequencies[None, :] % sample_count
    angles = phase_index.astype(jnp.float32) * (2.0 * math.pi / sample_count)
    pairs = jnp.stack([jnp.cos(angles), -jnp.sin(angles)], axis=2).reshape(
        sample_count, 2 * harm_count
    )
    forward = pairs / math.sqrt(harm_count)
    backward = pairs.T / math.sqrt(sample_count)
    return (forward, backward)


def normal_sum(iterate, below_edge, above_edge):
    low_side = jnp.concatenate([below_edge, iterate[..., :-1]], axis=-1)
    high_side = jnp.concatenate([iterate[..., 1:], above_edge], axis=-1)
    return low_side + high_side


def relax(source, base_rate, frequency, beside):
    var_count = base_rate.shape[0]
    numerator = source + coupling * beside
    num_real = numerator[:, :var_count]
    num_imag = numerator[:, var_count:]
    rate_col = frequency[:, None, None, None]
    denominator = base_rate * base_rate + rate_col * rate_col
    new_real = (num_real * base_rate + num_imag * rate_col) / denominator
    new_imag = (num_imag * base_rate - num_real * rate_col) / denominator
    return jnp.concatenate([new_real, new_imag], axis=1)


def correction_terms(iterate, previous):
    var_count = previous.shape[1] // 2
    old_real = previous[:, :var_count]
    old_imag = previous[:, var_count:]
    it_real = iterate[:, :var_count]
    it_imag = iterate[:, var_count:]
    proj_real = jnp.sum(old_real * it_real + old_imag * it_imag, axis=(1, 2, 3))
    proj_imag = jnp.sum(old_real * it_imag - old_imag * it_real, axis=(1, 2, 3))
    norm_old = jnp.sum(old_real * old_real + old_imag * old_imag, axis=(1, 2, 3))
    return (proj_real, proj_imag, norm_old)


def apply_correction(iterate, previous, totals):
    proj_real, proj_imag, norm_old = totals
    var_count = previous.shape[1] // 2
    old_real = previous[:, :var_count]
    old_imag = previous[:, var_count:]
    shift_real = ((proj_real - norm_old) / norm_old)[:, None, None, None]
    shift_imag = (proj_imag / norm_old)[:, None, None, None]
    new_real = iterate[:, :var_count] - (shift_real * old_real - shift_imag * old_imag)
    new_imag = iterate[:, var_count:] - (shift_real * old_imag + shift_imag * old_real)
    return jnp.concatenate([new_real, new_imag], axis=1)


def tile_sum(values):
    count = lax.axis_size(TILE)
    spread = jnp.broadcast_to(values[None], (count,) + values.shape)
    return lax.all_to_all(spread, TILE, 0, 0, tiled=True).sum(axis=0)


def spectral_slabs(field, forward, backward):
    harms, chans, rows, depth = field.shape
    groups = lax.axis_size("harm")
    width = depth // groups
    var_count = chans // 2
    cols = field.reshape(harms * chans * rows, depth).T.reshape(groups, width, harms * chans * rows)
    slabs = lax.all_to_all(cols, "harm", 0, 0, tiled=True)
    slabs = slabs.reshape(groups, width, harms, 2, var_count, rows)
    samples = jnp.einsum(
        "mshp,szhpvy->mvyz",
        forward.reshape(forward.shape[0], groups, harms, 2),
        slabs,
        precision=lax.Precision.HIGHEST,
        preferred_element_type=jnp.float32,
    )
    product = jnp.roll(samples, -1, axis=1) * jnp.roll(samples, -2, axis=1)
    folded = jnp.einsum(
        "shpm,mvyz->szhpvy",
        backward.reshape(groups, harms, 2, backward.shape[1]),
        product,
        precision=lax.Precision.HIGHEST,
        preferred_element_type=jnp.float32,
    )
    back = lax.all_to_all(folded.reshape(groups, width, harms * chans * rows), "harm", 0, 0, tiled=True)
    return back.reshape(depth, harms * chans * rows).T.reshape(harms, chans, rows, depth)


def span_halo(blocks, width):
    count = lax.axis_size(TILE)
    rows = [block.shape[-2] for block in blocks]
    if len(blocks) == 1:
        low, high = blocks[0][..., rows[0] - width :, :], blocks[0][..., :width, :]
        return [
            (
                lax.ppermute(low, TILE, [(i, (i + 1) % count) for i in range(count)]),
                lax.ppermute(high, TILE, [((i + 1) % count, i) for i in range(count)]),
            )
        ]
    lows = jnp.concatenate([b[..., r - width :, :].reshape(-1) for b, r in zip(blocks, rows)])
    highs = jnp.concatenate([b[..., :width, :].reshape(-1) for b in blocks])
    from_left = lax.ppermute(lows, TILE, [(i, (i + 1) % count) for i in range(count)])
    from_right = lax.ppermute(highs, TILE, [((i + 1) % count, i) for i in range(count)])
    halos, offset = [], 0
    for b in blocks:
        shape = b.shape[:-2] + (width,) + b.shape[-1:]
        size = math.prod(shape)
        halos.append((from_left[offset : offset + size].reshape(shape), from_right[offset : offset + size].reshape(shape)))
        offset += size
    return halos


def with_halo(block, halo):
    return jnp.concatenate([halo[0], block, halo[1]], axis=-2)


def sweep(iterate, source, base_rate, keep, frequency):
    center = iterate[:, :, 1:-1]
    beside = iterate[:, :, :-2] + iterate[:, :, 2:]
    beside = beside + normal_sum(center, center[..., :1] * keep, jnp.zeros_like(center[..., :1]))
    return relax(source, base_rate, frequency, beside)


def conj_gain(values, base_rate, frequency):
    var_count = base_rate.shape[0]
    rate_col = frequency[:, None, None, None]
    denominator = base_rate * base_rate + rate_col * rate_col
    real, imag = values[:, :var_count], values[:, var_count:]
    return jnp.concatenate(
        [(real * base_rate - imag * rate_col) / denominator, (imag * base_rate + real * rate_col) / denominator],
        axis=1,
    )


def adjoint_weights(q_ext, base_ext, keep_ext, frequency, rows):
    total = rows + 2 * SWEEPS
    weights = [q_ext]
    for step in range(1, SWEEPS + 1):
        low, high = step - 1, total - step + 1
        scaled = conj_gain(weights[-1], base_ext[:, low:high], frequency)
        center = scaled[:, :, 1:-1]
        beside = scaled[:, :, :-2] + scaled[:, :, 2:]
        beside = beside + normal_sum(
            center, center[..., :1] * keep_ext[:, :, step : total - step], jnp.zeros_like(center[..., :1])
        )
        weights.append(coupling * beside)
    local = [w[:, :, SWEEPS - j : SWEEPS - j + rows] for j, w in enumerate(weights)]
    summed = local[0]
    for w in local[1:SWEEPS]:
        summed = summed + w
    return local[SWEEPS], conj_gain(summed, base_ext[:, SWEEPS : SWEEPS + rows], frequency)


def shards(q_old, base_rate, freq_table, wall_flags):
    forward, backward = build_tables(freq_table)
    frequency_all = freq_table.astype(jnp.float32) * (frequency_scale / freq_table.shape[0])
    harm_rank = lax.axis_index("harm")
    local_harms = q_old.shape[0]
    frequency = lax.dynamic_slice_in_dim(frequency_all, harm_rank * local_harms, local_harms)
    rows = q_old.shape[2]
    assert rows >= SWEEPS
    keep = (1 - wall_flags).astype(jnp.float32)[:, None]
    q_halo, base_halo, keep_halo = span_halo((q_old, base_rate, keep), SWEEPS)
    keep_ext = with_halo(keep, keep_halo)[None, None]
    base_ext = with_halo(base_rate, base_halo)
    q_ext = with_halo(q_old, q_halo)
    field_weight, source_weight = adjoint_weights(
        *lax.optimization_barrier((q_ext, base_ext, keep_ext, frequency)), rows
    )
    norm_old = correction_terms(q_old, q_old)[2]
    field_weight, source_weight, norm_old = lax.optimization_barrier((field_weight, source_weight, norm_old))
    field = q_old
    field_ext = q_ext
    for outer_step in range(ITERS):
        field_proj = correction_terms(field, field_weight)
        forcing = spectral_slabs(field, forward, backward)
        source_proj = correction_terms(marching * q_old + forcing_gain * forcing, source_weight)
        totals = tile_sum(
            jnp.stack([field_proj[0] + source_proj[0], field_proj[1] + source_proj[1], norm_old])
        )
        forcing_ext = with_halo(forcing, span_halo((forcing,), SWEEPS - 1)[0])
        source_ext = marching * q_ext[:, :, 1:-1] + forcing_gain * forcing_ext
        iterate = field_ext
        for sweep_step in range(1, SWEEPS + 1):
            low, high = sweep_step, rows + 2 * SWEEPS - sweep_step
            iterate = sweep(
                iterate,
                source_ext[:, :, low - 1 : high - 1],
                base_ext[:, low:high],
                keep_ext[:, :, low:high],
                frequency,
            )
        last = outer_step == ITERS - 1
        if not last:
            (it_halo,) = span_halo((iterate,), SWEEPS)
        field = apply_correction(iterate, q_old, totals)
        if not last:
            field_ext = jnp.concatenate(
                [
                    apply_correction(it_halo[0], q_halo[0], totals),
                    field,
                    apply_correction(it_halo[1], q_halo[1], totals),
                ],
                axis=2,
            )
    return field


def solution(mesh):
    harms, tiles = mesh.devices.shape
    split = Mesh(mesh.devices.reshape(harms, tiles // 2, 2), ("harm", "z", "core"))
    placed = (P("harm", None, TILE, None), P(None, TILE, None), P(), P(TILE))
    return jax.shard_map(
        shards, mesh=split, in_specs=placed, out_specs=P("harm", None, TILE, None), check_vma=False
    )
```

```python
import math

import jax
import jax.numpy as jnp
from jax import lax
from jax.sharding import Mesh, PartitionSpec as P


ITERS = 2
SWEEPS = 4
TILE = ("z", "core")


coupling = 0.24
forcing_gain = 0.5
marching = 1.0
frequency_scale = 0.5


def build_tables(frequencies):
    harm_count = frequencies.shape[0]
    sample_count = 2 * harm_count
    sample_index = jnp.arange(sample_count, dtype=jnp.int32)
    phase_index = sample_index[:, None] * frequencies[None, :] % sample_count
    angles = phase_index.astype(jnp.float32) * (2.0 * math.pi / sample_count)
    pairs = jnp.stack([jnp.cos(angles), -jnp.sin(angles)], axis=2).reshape(
        sample_count, 2 * harm_count
    )
    forward = pairs / math.sqrt(harm_count)
    backward = pairs.T / math.sqrt(sample_count)
    return (forward, backward)


def normal_sum(iterate, below_edge, above_edge):
    low_side = jnp.concatenate([below_edge, iterate[..., :-1]], axis=-1)
    high_side = jnp.concatenate([iterate[..., 1:], above_edge], axis=-1)
    return low_side + high_side


def relax(source, base_rate, frequency, beside):
    var_count = base_rate.shape[0]
    numerator = source + coupling * beside
    num_real = numerator[:, :var_count]
    num_imag = numerator[:, var_count:]
    rate_col = frequency[:, None, None, None]
    denominator = base_rate * base_rate + rate_col * rate_col
    new_real = (num_real * base_rate + num_imag * rate_col) / denominator
    new_imag = (num_imag * base_rate - num_real * rate_col) / denominator
    return jnp.concatenate([new_real, new_imag], axis=1)


def correction_terms(iterate, previous):
    var_count = previous.shape[1] // 2
    old_real = previous[:, :var_count]
    old_imag = previous[:, var_count:]
    it_real = iterate[:, :var_count]
    it_imag = iterate[:, var_count:]
    proj_real = jnp.sum(old_real * it_real + old_imag * it_imag, axis=(1, 2, 3))
    proj_imag = jnp.sum(old_real * it_imag - old_imag * it_real, axis=(1, 2, 3))
    norm_old = jnp.sum(old_real * old_real + old_imag * old_imag, axis=(1, 2, 3))
    return (proj_real, proj_imag, norm_old)


def apply_correction(iterate, previous, totals):
    proj_real, proj_imag, norm_old = totals
    var_count = previous.shape[1] // 2
    old_real = previous[:, :var_count]
    old_imag = previous[:, var_count:]
    shift_real = ((proj_real - norm_old) / norm_old)[:, None, None, None]
    shift_imag = (proj_imag / norm_old)[:, None, None, None]
    new_real = iterate[:, :var_count] - (shift_real * old_real - shift_imag * old_imag)
    new_imag = iterate[:, var_count:] - (shift_real * old_imag + shift_imag * old_real)
    return jnp.concatenate([new_real, new_imag], axis=1)


def tile_sum(values):
    count = lax.axis_size(TILE)
    spread = jnp.broadcast_to(values[None], (count,) + values.shape)
    return lax.all_to_all(spread, TILE, 0, 0, tiled=True).sum(axis=0)


def spectral_slabs(field, forward, backward):
    harms, chans, rows, depth = field.shape
    groups = lax.axis_size("harm")
    width = depth // groups
    var_count = chans // 2
    cols = field.reshape(harms * chans * rows, depth).T.reshape(groups, width, harms * chans * rows)
    slabs = lax.all_to_all(cols, "harm", 0, 0, tiled=True)
    slabs = slabs.reshape(groups, width, harms, 2, var_count, rows)
    samples = jnp.einsum(
        "mshp,szhpvy->mvyz",
        forward.reshape(forward.shape[0], groups, harms, 2),
        slabs,
        precision=lax.Precision.HIGHEST,
        preferred_element_type=jnp.float32,
    )
    product = jnp.roll(samples, -1, axis=1) * jnp.roll(samples, -2, axis=1)
    folded = jnp.einsum(
        "shpm,mvyz->szhpvy",
        backward.reshape(groups, harms, 2, backward.shape[1]),
        product,
        precision=lax.Precision.HIGHEST,
        preferred_element_type=jnp.float32,
    )
    back = lax.all_to_all(folded.reshape(groups, width, harms * chans * rows), "harm", 0, 0, tiled=True)
    back = back.reshape(depth, harms * chans * rows)
    return back.T.reshape(harms, chans, rows, depth), back.reshape(depth, harms, chans, rows)


def lane_terms(weight, values):
    var_count = weight.shape[2] // 2
    w_real, w_imag = weight[:, :, :var_count], weight[:, :, var_count:]
    v_real, v_imag = values[:, :, :var_count], values[:, :, var_count:]
    proj_real = jnp.sum(w_real * v_real + w_imag * v_imag, axis=(0, 2, 3))
    proj_imag = jnp.sum(w_real * v_imag - w_imag * v_real, axis=(0, 2, 3))
    return proj_real, proj_imag


def span_halo(blocks, width):
    count = lax.axis_size(TILE)
    rows = [block.shape[-2] for block in blocks]
    if len(blocks) == 1:
        low, high = blocks[0][..., rows[0] - width :, :], blocks[0][..., :width, :]
        return [
            (
                lax.ppermute(low, TILE, [(i, (i + 1) % count) for i in range(count)]),
                lax.ppermute(high, TILE, [((i + 1) % count, i) for i in range(count)]),
            )
        ]
    lows = jnp.concatenate([b[..., r - width :, :].reshape(-1) for b, r in zip(blocks, rows)])
    highs = jnp.concatenate([b[..., :width, :].reshape(-1) for b in blocks])
    from_left = lax.ppermute(lows, TILE, [(i, (i + 1) % count) for i in range(count)])
    from_right = lax.ppermute(highs, TILE, [((i + 1) % count, i) for i in range(count)])
    halos, offset = [], 0
    for b in blocks:
        shape = b.shape[:-2] + (width,) + b.shape[-1:]
        size = math.prod(shape)
        halos.append((from_left[offset : offset + size].reshape(shape), from_right[offset : offset + size].reshape(shape)))
        offset += size
    return halos


def with_halo(block, halo):
    return jnp.concatenate([halo[0], block, halo[1]], axis=-2)


def sweep(iterate, source, base_rate, keep, frequency):
    center = iterate[:, :, 1:-1]
    beside = iterate[:, :, :-2] + iterate[:, :, 2:]
    beside = beside + normal_sum(center, center[..., :1] * keep, jnp.zeros_like(center[..., :1]))
    return relax(source, base_rate, frequency, beside)


def conj_gain(values, base_rate, frequency):
    var_count = base_rate.shape[0]
    rate_col = frequency[:, None, None, None]
    denominator = base_rate * base_rate + rate_col * rate_col
    real, imag = values[:, :var_count], values[:, var_count:]
    return jnp.concatenate(
        [(real * base_rate - imag * rate_col) / denominator, (imag * base_rate + real * rate_col) / denominator],
        axis=1,
    )


def adjoint_weights(q_ext, base_ext, keep_ext, frequency, rows):
    total = rows + 2 * SWEEPS
    weights = [q_ext]
    for step in range(1, SWEEPS + 1):
        low, high = step - 1, total - step + 1
        scaled = conj_gain(weights[-1], base_ext[:, low:high], frequency)
        center = scaled[:, :, 1:-1]
        beside = scaled[:, :, :-2] + scaled[:, :, 2:]
        beside = beside + normal_sum(
            center, center[..., :1] * keep_ext[:, :, step : total - step], jnp.zeros_like(center[..., :1])
        )
        weights.append(coupling * beside)
    local = [w[:, :, SWEEPS - j : SWEEPS - j + rows] for j, w in enumerate(weights)]
    summed = local[0]
    for w in local[1:SWEEPS]:
        summed = summed + w
    return local[SWEEPS], conj_gain(summed, base_ext[:, SWEEPS : SWEEPS + rows], frequency)


def shards(q_old, base_rate, freq_table, wall_flags):
    forward, backward = build_tables(freq_table)
    frequency_all = freq_table.astype(jnp.float32) * (frequency_scale / freq_table.shape[0])
    harm_rank = lax.axis_index("harm")
    local_harms = q_old.shape[0]
    frequency = lax.dynamic_slice_in_dim(frequency_all, harm_rank * local_harms, local_harms)
    rows = q_old.shape[2]
    assert rows >= SWEEPS
    keep = (1 - wall_flags).astype(jnp.float32)[:, None]
    q_halo, base_halo, keep_halo = span_halo((q_old, base_rate, keep), SWEEPS)
    keep_ext = with_halo(keep, keep_halo)[None, None]
    base_ext = with_halo(base_rate, base_halo)
    q_ext = with_halo(q_old, q_halo)
    field_weight, source_weight = adjoint_weights(
        *lax.optimization_barrier((q_ext, base_ext, keep_ext, frequency)), rows
    )
    norm_old = correction_terms(q_old, q_old)[2]
    old_proj = correction_terms(q_old, source_weight)[:2]
    harms, chans, _, depth = q_old.shape
    lane_weight = source_weight.reshape(harms * chans * rows, depth).T.reshape(depth, harms, chans, rows)
    field_weight, lane_weight, norm_old, old_proj = lax.optimization_barrier(
        (field_weight, lane_weight, norm_old, old_proj)
    )
    field = q_old
    field_ext = q_ext
    for outer_step in range(ITERS):
        field_proj = correction_terms(field, field_weight)
        forcing, forcing_lanes = spectral_slabs(field, forward, backward)
        forced_proj = lane_terms(lane_weight, forcing_lanes)
        source_proj = [marching * o + forcing_gain * f for o, f in zip(old_proj, forced_proj)]
        totals = tile_sum(
            jnp.stack([field_proj[0] + source_proj[0], field_proj[1] + source_proj[1], norm_old])
        )
        forcing_ext = with_halo(forcing, span_halo((forcing,), SWEEPS - 1)[0])
        source_ext = marching * q_ext[:, :, 1:-1] + forcing_gain * forcing_ext
        iterate = field_ext
        for sweep_step in range(1, SWEEPS + 1):
            low, high = sweep_step, rows + 2 * SWEEPS - sweep_step
            iterate = sweep(
                iterate,
                source_ext[:, :, low - 1 : high - 1],
                base_ext[:, low:high],
                keep_ext[:, :, low:high],
                frequency,
            )
        last = outer_step == ITERS - 1
        if not last:
            (it_halo,) = span_halo((iterate,), SWEEPS)
        field = apply_correction(iterate, q_old, totals)
        if not last:
            field_ext = jnp.concatenate(
                [
                    apply_correction(it_halo[0], q_halo[0], totals),
                    field,
                    apply_correction(it_halo[1], q_halo[1], totals),
                ],
                axis=2,
            )
    return field


def solution(mesh):
    harms, tiles = mesh.devices.shape
    split = Mesh(mesh.devices.reshape(harms, tiles // 2, 2), ("harm", "z", "core"))
    placed = (P("harm", None, TILE, None), P(None, TILE, None), P(), P(TILE))
    return jax.shard_map(
        shards, mesh=split, in_specs=placed, out_specs=P("harm", None, TILE, None), check_vma=False
    )
```

```python
import math

import jax
import jax.numpy as jnp
from jax import lax
from jax.sharding import Mesh, PartitionSpec as P


ITERS = 2
SWEEPS = 4
TILE = ("z", "core")


coupling = 0.24
forcing_gain = 0.5
marching = 1.0
frequency_scale = 0.5


def build_tables(frequencies):
    harm_count = frequencies.shape[0]
    sample_count = 2 * harm_count
    sample_index = jnp.arange(sample_count, dtype=jnp.int32)
    phase_index = sample_index[:, None] * frequencies[None, :] % sample_count
    angles = phase_index.astype(jnp.float32) * (2.0 * math.pi / sample_count)
    pairs = jnp.stack([jnp.cos(angles), -jnp.sin(angles)], axis=2).reshape(
        sample_count, 2 * harm_count
    )
    forward = pairs / math.sqrt(harm_count)
    backward = pairs.T / math.sqrt(sample_count)
    return (forward, backward)


def normal_sum(iterate, below_edge, above_edge):
    low_side = jnp.concatenate([below_edge, iterate[..., :-1]], axis=-1)
    high_side = jnp.concatenate([iterate[..., 1:], above_edge], axis=-1)
    return low_side + high_side


def relax(source, base_rate, frequency, beside):
    var_count = base_rate.shape[0]
    numerator = source + coupling * beside
    num_real = numerator[:, :var_count]
    num_imag = numerator[:, var_count:]
    rate_col = frequency[:, None, None, None]
    denominator = base_rate * base_rate + rate_col * rate_col
    new_real = (num_real * base_rate + num_imag * rate_col) / denominator
    new_imag = (num_imag * base_rate - num_real * rate_col) / denominator
    return jnp.concatenate([new_real, new_imag], axis=1)


def correction_terms(iterate, previous):
    var_count = previous.shape[1] // 2
    old_real = previous[:, :var_count]
    old_imag = previous[:, var_count:]
    it_real = iterate[:, :var_count]
    it_imag = iterate[:, var_count:]
    proj_real = jnp.sum(old_real * it_real + old_imag * it_imag, axis=(1, 2, 3))
    proj_imag = jnp.sum(old_real * it_imag - old_imag * it_real, axis=(1, 2, 3))
    norm_old = jnp.sum(old_real * old_real + old_imag * old_imag, axis=(1, 2, 3))
    return (proj_real, proj_imag, norm_old)


def apply_correction(iterate, previous, totals):
    proj_real, proj_imag, norm_old = totals
    var_count = previous.shape[1] // 2
    old_real = previous[:, :var_count]
    old_imag = previous[:, var_count:]
    shift_real = ((proj_real - norm_old) / norm_old)[:, None, None, None]
    shift_imag = (proj_imag / norm_old)[:, None, None, None]
    new_real = iterate[:, :var_count] - (shift_real * old_real - shift_imag * old_imag)
    new_imag = iterate[:, var_count:] - (shift_real * old_imag + shift_imag * old_real)
    return jnp.concatenate([new_real, new_imag], axis=1)


def tile_sum(values):
    count = lax.axis_size(TILE)
    spread = jnp.broadcast_to(values[None], (count,) + values.shape)
    return lax.all_to_all(spread, TILE, 0, 0, tiled=True).sum(axis=0)


def spectral_slabs(field, forward, backward):
    harms, chans, rows, depth = field.shape
    groups = lax.axis_size("harm")
    width = depth // groups
    var_count = chans // 2
    cols = field.reshape(harms * chans * rows, depth).T.reshape(groups, width, harms * chans * rows)
    slabs = lax.all_to_all(cols, "harm", 0, 0, tiled=True)
    slabs = slabs.reshape(groups, width, harms, 2, var_count, rows)
    samples = jnp.einsum(
        "mshp,szhpvy->mvyz",
        forward.reshape(forward.shape[0], groups, harms, 2),
        slabs,
        precision=lax.Precision.HIGHEST,
        preferred_element_type=jnp.float32,
    )
    product = jnp.roll(samples, -1, axis=1) * jnp.roll(samples, -2, axis=1)
    folded = jnp.einsum(
        "shpm,mvyz->szhpvy",
        backward.reshape(groups, harms, 2, backward.shape[1]),
        product,
        precision=lax.Precision.HIGHEST,
        preferred_element_type=jnp.float32,
    )
    back = lax.all_to_all(folded.reshape(groups, width, harms * chans * rows), "harm", 0, 0, tiled=True)
    return back.reshape(depth, harms * chans * rows).T.reshape(harms, chans, rows, depth)


def span_halo(blocks, width):
    count = lax.axis_size(TILE)
    rows = [block.shape[-2] for block in blocks]
    if len(blocks) == 1:
        low, high = blocks[0][..., rows[0] - width :, :], blocks[0][..., :width, :]
        return [
            (
                lax.ppermute(low, TILE, [(i, (i + 1) % count) for i in range(count)]),
                lax.ppermute(high, TILE, [((i + 1) % count, i) for i in range(count)]),
            )
        ]
    lows = jnp.concatenate([b[..., r - width :, :].reshape(-1) for b, r in zip(blocks, rows)])
    highs = jnp.concatenate([b[..., :width, :].reshape(-1) for b in blocks])
    from_left = lax.ppermute(lows, TILE, [(i, (i + 1) % count) for i in range(count)])
    from_right = lax.ppermute(highs, TILE, [((i + 1) % count, i) for i in range(count)])
    halos, offset = [], 0
    for b in blocks:
        shape = b.shape[:-2] + (width,) + b.shape[-1:]
        size = math.prod(shape)
        halos.append((from_left[offset : offset + size].reshape(shape), from_right[offset : offset + size].reshape(shape)))
        offset += size
    return halos


def with_halo(block, halo):
    return jnp.concatenate([halo[0], block, halo[1]], axis=-2)


def sweep(iterate, source, base_rate, keep, frequency):
    center = iterate[:, :, 1:-1]
    beside = iterate[:, :, :-2] + iterate[:, :, 2:]
    beside = beside + normal_sum(center, center[..., :1] * keep, jnp.zeros_like(center[..., :1]))
    return relax(source, base_rate, frequency, beside)


def conj_gain(values, base_rate, frequency):
    var_count = base_rate.shape[0]
    rate_col = frequency[:, None, None, None]
    denominator = base_rate * base_rate + rate_col * rate_col
    real, imag = values[:, :var_count], values[:, var_count:]
    return jnp.concatenate(
        [(real * base_rate - imag * rate_col) / denominator, (imag * base_rate + real * rate_col) / denominator],
        axis=1,
    )


def adjoint_weights(q_ext, base_ext, keep_ext, frequency, rows):
    def step(_, carry):
        weight, summed = carry
        scaled = conj_gain(weight, base_ext, frequency)
        beside = jnp.roll(scaled, 1, axis=2) + jnp.roll(scaled, -1, axis=2)
        beside = beside + normal_sum(scaled, scaled[..., :1] * keep_ext, jnp.zeros_like(scaled[..., :1]))
        return coupling * beside, summed + weight

    weight, summed = lax.fori_loop(0, SWEEPS, step, (q_ext, jnp.zeros_like(q_ext)))
    local = slice(SWEEPS, SWEEPS + rows)
    return weight[:, :, local], conj_gain(summed[:, :, local], base_ext[:, local], frequency)


def shards(q_old, base_rate, freq_table, wall_flags):
    forward, backward = build_tables(freq_table)
    frequency_all = freq_table.astype(jnp.float32) * (frequency_scale / freq_table.shape[0])
    harm_rank = lax.axis_index("harm")
    local_harms = q_old.shape[0]
    frequency = lax.dynamic_slice_in_dim(frequency_all, harm_rank * local_harms, local_harms)
    rows = q_old.shape[2]
    assert rows >= SWEEPS
    keep = (1 - wall_flags).astype(jnp.float32)[:, None]
    q_halo, base_halo, keep_halo = span_halo((q_old, base_rate, keep), SWEEPS)
    keep_ext = with_halo(keep, keep_halo)[None, None]
    base_ext = with_halo(base_rate, base_halo)
    q_ext = with_halo(q_old, q_halo)
    field_weight, source_weight = adjoint_weights(
        *lax.optimization_barrier((q_ext, base_ext, keep_ext, frequency)), rows
    )
    norm_old = correction_terms(q_old, q_old)[2]
    field_weight, source_weight, norm_old = lax.optimization_barrier((field_weight, source_weight, norm_old))
    field = q_old
    field_ext = q_ext
    for outer_step in range(ITERS):
        field_proj = correction_terms(field, field_weight)
        forcing = spectral_slabs(field, forward, backward)
        source_proj = correction_terms(marching * q_old + forcing_gain * forcing, source_weight)
        totals = tile_sum(
            jnp.stack([field_proj[0] + source_proj[0], field_proj[1] + source_proj[1], norm_old])
        )
        forcing_ext = with_halo(forcing, span_halo((forcing,), SWEEPS - 1)[0])
        source_ext = marching * q_ext[:, :, 1:-1] + forcing_gain * forcing_ext
        iterate = field_ext
        for sweep_step in range(1, SWEEPS + 1):
            low, high = sweep_step, rows + 2 * SWEEPS - sweep_step
            iterate = sweep(
                iterate,
                source_ext[:, :, low - 1 : high - 1],
                base_ext[:, low:high],
                keep_ext[:, :, low:high],
                frequency,
            )
        last = outer_step == ITERS - 1
        if not last:
            (it_halo,) = span_halo((iterate,), SWEEPS)
        field = apply_correction(iterate, q_old, totals)
        if not last:
            field_ext = jnp.concatenate(
                [
                    apply_correction(it_halo[0], q_halo[0], totals),
                    field,
                    apply_correction(it_halo[1], q_halo[1], totals),
                ],
                axis=2,
            )
    return field


def solution(mesh):
    harms, tiles = mesh.devices.shape
    split = Mesh(mesh.devices.reshape(harms, tiles // 2, 2), ("harm", "z", "core"))
    placed = (P("harm", None, TILE, None), P(None, TILE, None), P(), P(TILE))
    return jax.shard_map(
        shards, mesh=split, in_specs=placed, out_specs=P("harm", None, TILE, None), check_vma=False
    )
```
